32 devices in a mesh: blk: 4 (over z), rows: 8 (over y, x, core).
Axes of the slice: x: 2, y: 2, z: 4, core: 2. Of those that a mesh axis runs over, the one named last changes fastest.
Arguments:
- features: bfloat16 [4, 4096, 2048], P(None, ('blk', 'rows')), may hold values from -6 to 6
- owner_ids: int32 [4096, 1], P(('blk', 'rows')), may hold values from 0 to 7; in each aligned block of 128 rows (0 to 127, 128 to 255, ...) at most 32 rows name the same one
- test_blocks: bfloat16 [4, 192, 2048], P(None, 'blk'), may hold values from -0.0625 to 0.0625
Outputs:
- scores: bfloat16 [8192, 192], P(('blk', 'rows'))
The draws below stay inside these ranges and needn't reach their ends.
Inputs may be any that keep to these rules, and one draw needn't show every extreme that they name: `owner_ids`: within each aligned block of 128 rows (the rows of one device) no owner is named more than 32 times.
All inputs are finite; a program needn't handle non-finite values.
Results may differ from the reference program's by a relative error of at most 0.001.
Values may be sent and summed in bfloat16 or wider, within the bound.
No kernel may reach another device: no remote copies, remote signals or barrier semaphores. Data moves between devices by JAX's collectives and lax.ppermute only.
A program may use at most 128 MiB of HBM per device.

```python
import math
import jax
import jax.numpy as jnp
import numpy as np

K = 2048
R = 4
S = 128
CAP = 32
TRAIN = 4096
TESTS = 192
SLOTS = 8192
N_BLK = 4
N_ROWS = 8


def block_levels(key, shape, pieces, smallest, high):
    loudness = 1.0
    for dim, parts in pieces:
        heights = jax.random.uniform(jax.random.fold_in(jax.random.fold_in(key, 6), dim), (parts,), jnp.float32, smallest / len(pieces), high / len(pieces))
        loudness = loudness * jnp.repeat(jnp.exp(heights), shape[dim] // parts).reshape((-1,) + (1,) * (len(shape) - 1 - dim))
    return loudness


def shared_out(own_key, own, number, rows, number_of, top, bound, lean):
    ranking = jax.random.permutation(own_key, number_of)
    heavy_load, ordinary = shares(number_of, rows * top, bound, lean, True), shares(number_of, rows * top, bound, lean, False)
    places = jnp.arange(number_of)

    def named(lengths, turn):
        used = int((lengths > 0).sum())
        fixed = max(1, used // 4)
        shifted = fixed + (places - fixed + turn * (used - fixed)) % max(1, number_of - fixed)
        return jnp.zeros((number_of,), jnp.int32).at[ranking[jnp.where(places < fixed, places, shifted)]].set(jnp.asarray(lengths, jnp.int32))

    lengths = jnp.where(number % 4 == 0, named(heavy_load, number // 4), named(ordinary, number - number // 4 - 1))
    mixed = jax.random.permutation(jax.random.fold_in(own, 3), number_of)
    source_of, receiver = mixed[0:number_of // 2 * 2:2], mixed[1:number_of // 2 * 2:2]
    room = jnp.minimum(lengths[source_of] - 1, bound - lengths[receiver]) // 2
    room = jnp.where((source_of == ranking[0]) | (receiver == ranking[0]) | (lengths[receiver] == 0), 0, jnp.maximum(room, 0))
    shifted = jax.random.randint(jax.random.fold_in(own, 4), (number_of // 2,), 0, 1 << 20) % (room + 1)
    lengths = lengths.at[source_of].add(-shifted).at[receiver].add(shifted)
    members = jnp.searchsorted(jnp.cumsum(lengths), jnp.arange(rows * top), side="right").astype(jnp.int32)
    listing = members.reshape(top, rows).T
    listing = listing[jax.random.permutation(jax.random.fold_in(own, 1), rows)]
    turn = jax.random.randint(jax.random.fold_in(own, 2), (rows, 1), 0, top)
    return jnp.take_along_axis(listing, (jnp.arange(top)[None, :] + turn) % top, axis=1)


def shares(count, total, most, lean, full):
    portions = [(1 << 20) // math.isqrt(standing ** lean) + 1 for standing in range(1, count + 1)]
    largest = most if full else min(most, max(-(-total // count), total * portions[0] // sum(portions)))
    least = 1 if total - largest >= count - 1 else 0
    counts, surplus = [largest] + [least] * (count - 1), total - largest - least * (count - 1)
    while surplus > 0:
        movable = [i for i in range(1, count) if counts[i] < largest] or [i for i in range(1, count) if counts[i] < most]
        mass, remaining = sum([portions[i] for i in movable]), surplus
        for i in movable:
            extra = min(most - counts[i], max(1, remaining * portions[i] // mass), surplus)
            counts[i] = counts[i] + extra
            surplus = surplus - extra
    return np.array(counts)


def centred(own_key, shape, scale, bound, pieces=(), kind=jnp.bfloat16):
    drawn = scale * jax.random.normal(own_key, shape, jnp.float32)
    if pieces:
        drawn = drawn * block_levels(own_key, shape, pieces, -0.22, 0.18)
    return jnp.clip(drawn, -bound, bound).astype(kind)


def setup_inputs(seed: int = 0) -> dict:
    key_of = jax.random.split(jax.random.key(seed), 4)
    features = centred(key_of[0], (R, TRAIN, K), 1.0, 6.0, ((1, 32),))
    owner_ids_keys = jax.random.split(jax.random.fold_in(key_of[1], 1), TRAIN // S)
    owner_ids_turns = jax.random.permutation(jax.random.fold_in(key_of[1], 3), TRAIN // S)
    owner_ids = jax.vmap(lambda own, number: shared_out(jax.random.fold_in(key_of[1], 2), own, number, S, N_ROWS, 1, CAP, 2))(owner_ids_keys, owner_ids_turns).reshape((TRAIN, 1))
    test_blocks = centred(key_of[2], (R, TESTS, K), (R * K) ** -0.5, 0.0625, ((1, 4),))
    return dict(features=features, owner_ids=owner_ids, test_blocks=test_blocks)


def reference(features, owner_ids, test_blocks):
    total = jnp.zeros((features.shape[1], test_blocks.shape[1]), jnp.float32)
    for run in range(R):
        total = total + jnp.dot(features[run], test_blocks[run].T, preferred_element_type=jnp.float32)
    row_scores = total.astype(jnp.bfloat16)
    groups = N_BLK * N_ROWS
    owner = owner_ids[:, 0].reshape(groups, S).astype(jnp.int32)
    onehot = (owner[:, :, None] == jnp.arange(N_ROWS, dtype=jnp.int32)[None, None, :]).astype(jnp.int32)
    before = jnp.cumsum(onehot, axis=1) - onehot
    rank = jnp.sum(before * onehot, axis=2).astype(jnp.int32)
    group_ids = jnp.arange(groups, dtype=jnp.int32)[:, None]
    block_ids = group_ids // N_ROWS
    source = group_ids % N_ROWS
    dest = (((block_ids * N_ROWS + owner) * N_ROWS + source) * CAP + rank).astype(jnp.int32)
    scores = jnp.zeros((SLOTS, test_blocks.shape[1]), jnp.bfloat16)
    return scores.at[dest.reshape(-1)].set(row_scores)
```

```python
import jax
import jax.numpy as jnp
from jax import lax
from jax.sharding import PartitionSpec as P


def slot_matrix(owner_ids, owners_n, capacity):
    owner = owner_ids[:, 0]
    onehot = (owner[:, None] == jnp.arange(owners_n, dtype=jnp.int32)[None, :]).astype(jnp.int32)
    before = jnp.cumsum(onehot, axis=0) - onehot
    rank = jnp.sum(before * onehot, axis=1)
    slot = owner * capacity + rank
    slots = jnp.arange(owners_n * capacity, dtype=jnp.int32)
    return (slots[:, None] == slot[None, :]).astype(jnp.bfloat16)


def on_device(features, owner_ids, test_blocks):
    owners_n = lax.axis_size("rows")
    local_rows = features.shape[1]
    capacity = 2 * local_rows // owners_n
    tests = lax.all_gather(test_blocks, "blk", axis=1, tiled=True)
    total = jnp.einsum("rsk,rtk->st", features, tests, preferred_element_type=jnp.float32)
    row_scores = total.astype(jnp.bfloat16)
    placed = jnp.dot(
        slot_matrix(owner_ids, owners_n, capacity), row_scores, preferred_element_type=jnp.float32
    ).astype(jnp.bfloat16)
    return lax.all_to_all(placed, "rows", split_axis=0, concat_axis=0, tiled=True)


def solution(mesh):
    return jax.shard_map(
        on_device,
        mesh=mesh,
        in_specs=(P(None, ("blk", "rows"), None), P(("blk", "rows"), None), P(None, "blk", None)),
        out_specs=P(("blk", "rows"), None),
        check_vma=False,
    )
```

```python
import jax
import jax.numpy as jnp
from jax import lax
from jax.sharding import PartitionSpec as P


def slot_matrix(owner_ids, owners_n, capacity):
    owner = owner_ids[:, 0]
    onehot = (owner[:, None] == jnp.arange(owners_n, dtype=jnp.int32)[None, :]).astype(jnp.int32)
    before = jnp.cumsum(onehot, axis=0) - onehot
    rank = jnp.sum(before * onehot, axis=1)
    slot = owner * capacity + rank
    slots = jnp.arange(owners_n * capacity, dtype=jnp.int32)
    return (slots[:, None] == slot[None, :]).astype(jnp.bfloat16)


def plane_bits(owners_n):
    bits = [i for i in range(1, owners_n.bit_length() - 1)]
    return bits + [0] if owners_n > 1 else []


def gathered_pieces(test_blocks, chunk):
    blocks_n = lax.axis_size("blk")
    owners_n = lax.axis_size("rows")
    here = lax.axis_index("rows")
    piece = lax.dynamic_slice_in_dim(test_blocks, here * chunk, chunk, axis=2)
    arrived = []
    for step in range(1, blocks_n):
        pairs = [(b, (b - step) % blocks_n) for b in range(blocks_n)]
        arrived.append(lax.ppermute(piece, "blk", pairs))
    stack = jnp.concatenate(arrived, axis=1)[None]
    masks = [0]
    for bit in plane_bits(owners_n):
        pairs = [(s, s ^ (1 << bit)) for s in range(owners_n)]
        stack = jnp.concatenate([stack, lax.ppermute(stack, "rows", pairs)], axis=0)
        masks = masks + [m ^ (1 << bit) for m in masks]
    return stack, masks


def on_device(features, owner_ids, test_blocks):
    owners_n = lax.axis_size("rows")
    blocks_n = lax.axis_size("blk")
    local_rows = features.shape[1]
    width = test_blocks.shape[1]
    capacity = 2 * local_rows // owners_n
    chunk = features.shape[2] // owners_n
    here = lax.axis_index("rows")
    block = lax.axis_index("blk")
    stack, masks = gathered_pieces(test_blocks, chunk)
    own = jnp.einsum("rsk,rtk->st", features, test_blocks, preferred_element_type=jnp.float32)
    remote = None
    for j, mask in enumerate(masks):
        part = lax.dynamic_slice_in_dim(features, (here ^ mask) * chunk, chunk, axis=2)
        term = jnp.einsum("rsk,rtk->st", part, stack[j], preferred_element_type=jnp.float32)
        remote = term if remote is None else remote + term
    relative = jnp.concatenate([own, remote], axis=1)
    doubled = jnp.concatenate([relative, relative], axis=1)
    start = ((blocks_n - block) % blocks_n) * width
    total = lax.dynamic_slice_in_dim(doubled, start, blocks_n * width, axis=1)
    row_scores = total.astype(jnp.bfloat16)
    placed = jnp.dot(
        slot_matrix(owner_ids, owners_n, capacity), row_scores, preferred_element_type=jnp.float32
    ).astype(jnp.bfloat16)
    return lax.all_to_all(placed, "rows", split_axis=0, concat_axis=0, tiled=True)


def solution(mesh):
    return jax.shard_map(
        on_device,
        mesh=mesh,
        in_specs=(P(None, ("blk", "rows"), None), P(("blk", "rows"), None), P(None, "blk", None)),
        out_specs=P(("blk", "rows"), None),
        check_vma=False,
    )
```

```python
import jax
import jax.numpy as jnp
from jax import lax
from jax.sharding import PartitionSpec as P


def slot_matrix(owner_ids, owners_n, capacity):
    owner = owner_ids[:, 0]
    onehot = (owner[:, None] == jnp.arange(owners_n, dtype=jnp.int32)[None, :]).astype(jnp.int32)
    before = jnp.cumsum(onehot, axis=0) - onehot
    rank = jnp.sum(before * onehot, axis=1)
    slot = owner * capacity + rank
    slots = jnp.arange(owners_n * capacity, dtype=jnp.int32)
    return (slots[:, None] == slot[None, :]).astype(jnp.bfloat16)


def xor_pairs(count, mask):
    return [(s, s ^ mask) for s in range(count)]


def on_device(features, owner_ids, test_blocks):
    owners_n = lax.axis_size("rows")
    blocks_n = lax.axis_size("blk")
    local_rows = features.shape[1]
    width = test_blocks.shape[1]
    capacity = 2 * local_rows // owners_n
    chunk = features.shape[2] // owners_n
    here = lax.axis_index("rows")
    block = lax.axis_index("blk")

    def term(offset, size, tests):
        part = lax.dynamic_slice_in_dim(features, offset, size, axis=2)
        return jnp.einsum("rsk,rtk->st", part, tests, preferred_element_type=jnp.float32)

    piece = lax.dynamic_slice_in_dim(test_blocks, here * chunk, chunk, axis=2)
    arrived = []
    for step in range(1, blocks_n):
        pairs = [(b, (b - step) % blocks_n) for b in range(blocks_n)]
        arrived.append(lax.ppermute(piece, "blk", pairs))
    mine = jnp.concatenate(arrived, axis=1)
    own = jnp.einsum("rsk,rtk->st", features, test_blocks, preferred_element_type=jnp.float32)
    remote = term(here * chunk, chunk, mine)
    chip_bits = [1 << i for i in range(1, owners_n.bit_length() - 1)]
    if len(chip_bits) == 2:
        bx, by = chip_bits
        along_x = lax.ppermute(mine, "rows", xor_pairs(owners_n, bx))
        along_y = lax.ppermute(mine, "rows", xor_pairs(owners_n, by))
        remote = remote + term((here ^ bx) * chunk, chunk, along_x)
        remote = remote + term((here ^ by) * chunk, chunk, along_y)
        half = chunk // 2
        first = lax.ppermute(along_y[:, :, :half], "rows", xor_pairs(owners_n, bx))
        second = lax.ppermute(along_x[:, :, half:], "rows", xor_pairs(owners_n, by))
        corner = (here ^ bx ^ by) * chunk
        remote = remote + term(corner, half, first) + term(corner + half, half, second)
        diagonal = jnp.concatenate([first, second], axis=2)
        held = jnp.stack([mine, along_x, along_y, diagonal])
        masks = [0, bx, by, bx ^ by]
    else:
        held = mine[None]
        masks = [0]
        for mask in chip_bits:
            got = lax.ppermute(held, "rows", xor_pairs(owners_n, mask))
            for j, m in enumerate(masks):
                remote = remote + term((here ^ mask ^ m) * chunk, chunk, got[j])
            held = jnp.concatenate([held, got], axis=0)
            masks = masks + [m ^ mask for m in masks]
    if owners_n > 1:
        got = lax.ppermute(held, "rows", xor_pairs(owners_n, 1))
        for j, m in enumerate(masks):
            remote = remote + term((here ^ 1 ^ m) * chunk, chunk, got[j])
    relative = jnp.concatenate([own, remote], axis=1)
    doubled = jnp.concatenate([relative, relative], axis=1)
    start = ((blocks_n - block) % blocks_n) * width
    total = lax.dynamic_slice_in_dim(doubled, start, blocks_n * width, axis=1)
    row_scores = total.astype(jnp.bfloat16)
    placed = jnp.dot(
        slot_matrix(owner_ids, owners_n, capacity), row_scores, preferred_element_type=jnp.float32
    ).astype(jnp.bfloat16)
    return lax.all_to_all(placed, "rows", split_axis=0, concat_axis=0, tiled=True)


def solution(mesh):
    return jax.shard_map(
        on_device,
        mesh=mesh,
        in_specs=(P(None, ("blk", "rows"), None), P(("blk", "rows"), None), P(None, "blk", None)),
        out_specs=P(("blk", "rows"), None),
        check_vma=False,
    )
```

```python
import jax
import jax.numpy as jnp
from jax import lax
from jax.sharding import PartitionSpec as P


def slot_matrix(owner_ids, owners_n, capacity):
    owner = owner_ids[:, 0]
    onehot = (owner[:, None] == jnp.arange(owners_n, dtype=jnp.int32)[None, :]).astype(jnp.int32)
    before = jnp.cumsum(onehot, axis=0) - onehot
    rank = jnp.sum(before * onehot, axis=1)
    slot = owner * capacity + rank
    slots = jnp.arange(owners_n * capacity, dtype=jnp.int32)
    return (slots[:, None] == slot[None, :]).astype(jnp.bfloat16)


def xor_pairs(count, mask):
    return [(s, s ^ mask) for s in range(count)]


def on_device(features, owner_ids, test_blocks):
    owners_n = lax.axis_size("rows")
    blocks_n = lax.axis_size("blk")
    local_rows = features.shape[1]
    width = test_blocks.shape[1]
    capacity = 2 * local_rows // owners_n
    chunk = features.shape[2] // owners_n
    here = lax.axis_index("rows")
    block = lax.axis_index("blk")

    def term(offset, size, tests):
        part = lax.dynamic_slice_in_dim(features, offset, size, axis=2)
        return jnp.einsum("rsk,rtk->st", part, tests, preferred_element_type=jnp.float32)

    piece = lax.dynamic_slice_in_dim(test_blocks, here * chunk, chunk, axis=2)
    arrived = []
    for step in range(1, blocks_n):
        pairs = [(b, (b - step) % blocks_n) for b in range(blocks_n)]
        arrived.append(lax.ppermute(piece, "blk", pairs))
    mine = jnp.concatenate(arrived, axis=1)
    own = jnp.einsum("rsk,rtk->st", features, test_blocks, preferred_element_type=jnp.float32)
    mine, own = lax.optimization_barrier((mine, own))
    remote = term(here * chunk, chunk, mine)
    chip_bits = [1 << i for i in range(1, owners_n.bit_length() - 1)]
    if len(chip_bits) == 2:
        bx, by = chip_bits
        along_x = lax.ppermute(mine, "rows", xor_pairs(owners_n, bx))
        along_y = lax.ppermute(mine, "rows", xor_pairs(owners_n, by))
        sibling = lax.ppermute(jnp.stack([mine, along_x, along_y]), "rows", xor_pairs(owners_n, 1))
        half = chunk // 2
        first = lax.ppermute(along_y[:, :, :half], "rows", xor_pairs(owners_n, bx))
        second = lax.ppermute(along_x[:, :, half:], "rows", xor_pairs(owners_n, by))
        remote = remote + term((here ^ bx) * chunk, chunk, along_x)
        remote = remote + term((here ^ by) * chunk, chunk, along_y)
        corner = (here ^ bx ^ by) * chunk
        remote = remote + term(corner, half, first) + term(corner + half, half, second)
        diagonal = jnp.concatenate([first, second], axis=2)
        late = lax.ppermute(diagonal, "rows", xor_pairs(owners_n, 1))
        parts = jnp.stack(
            [lax.dynamic_slice_in_dim(features, (here ^ 1 ^ m) * chunk, chunk, axis=2) for m in (0, bx, by)]
        )
        remote = remote + jnp.einsum("jrsk,jrtk->st", parts, sibling, preferred_element_type=jnp.float32)
        remote = remote + term((here ^ 1 ^ bx ^ by) * chunk, chunk, late)
    else:
        held = mine[None]
        masks = [0]
        for mask in chip_bits + [1]:
            got = lax.ppermute(held, "rows", xor_pairs(owners_n, mask))
            for j, m in enumerate(masks):
                remote = remote + term((here ^ mask ^ m) * chunk, chunk, got[j])
            held = jnp.concatenate([held, got], axis=0)
            masks = masks + [m ^ mask for m in masks]
    relative = jnp.concatenate([own, remote], axis=1)
    doubled = jnp.concatenate([relative, relative], axis=1)
    start = ((blocks_n - block) % blocks_n) * width
    total = lax.dynamic_slice_in_dim(doubled, start, blocks_n * width, axis=1)
    row_scores = total.astype(jnp.bfloat16)
    placed = jnp.dot(
        slot_matrix(owner_ids, owners_n, capacity), row_scores, preferred_element_type=jnp.float32
    ).astype(jnp.bfloat16)
    return lax.all_to_all(placed, "rows", split_axis=0, concat_axis=0, tiled=True)


def solution(mesh):
    return jax.shard_map(
        on_device,
        mesh=mesh,
        in_specs=(P(None, ("blk", "rows"), None), P(("blk", "rows"), None), P(None, "blk", None)),
        out_specs=P(("blk", "rows"), None),
        check_vma=False,
    )
```

```python
import jax
import jax.numpy as jnp
from jax import lax
from jax.sharding import PartitionSpec as P


def slot_matrix(owner_ids, owners_n, capacity):
    owner = owner_ids[:, 0]
    onehot = (owner[:, None] == jnp.arange(owners_n, dtype=jnp.int32)[None, :]).astype(jnp.int32)
    before = jnp.cumsum(onehot, axis=0) - onehot
    rank = jnp.sum(before * onehot, axis=1)
    slot = owner * capacity + rank
    slots = jnp.arange(owners_n * capacity, dtype=jnp.int32)
    return (slots[:, None] == slot[None, :]).astype(jnp.bfloat16)


def xor_pairs(count, mask):
    return [(s, s ^ mask) for s in range(count)]


def on_device(features, owner_ids, test_blocks):
    owners_n = lax.axis_size("rows")
    blocks_n = lax.axis_size("blk")
    local_rows = features.shape[1]
    width = test_blocks.shape[1]
    capacity = 2 * local_rows // owners_n
    chunk = features.shape[2] // owners_n
    here = lax.axis_index("rows")
    block = lax.axis_index("blk")

    def term(offset, size, tests):
        part = lax.dynamic_slice_in_dim(features, offset, size, axis=2)
        return jnp.einsum("rsk,rtk->st", part, tests, preferred_element_type=jnp.float32)

    piece = lax.dynamic_slice_in_dim(test_blocks, here * chunk, chunk, axis=2)
    arrived = []
    for step in range(1, blocks_n):
        pairs = [(b, (b - step) % blocks_n) for b in range(blocks_n)]
        arrived.append(lax.ppermute(piece, "blk", pairs))
    mine = jnp.concatenate(arrived, axis=1)
    own = jnp.einsum("rsk,rtk->st", features, test_blocks, preferred_element_type=jnp.float32)
    mine, own = lax.optimization_barrier((mine, own))
    chip_bits = [1 << i for i in range(1, owners_n.bit_length() - 1)]
    if len(chip_bits) == 2:
        bx, by = chip_bits
        masks = [0, bx, by, bx ^ by]
        lent = jnp.stack(
            [lax.dynamic_slice_in_dim(features, (here ^ 1 ^ m) * chunk, chunk, axis=2) for m in masks]
        )
        lent = lax.ppermute(lent, "rows", xor_pairs(owners_n, 1))
        both = [
            jnp.concatenate(
                [lax.dynamic_slice_in_dim(features, (here ^ m) * chunk, chunk, axis=2), lent[j]], axis=1
            )
            for j, m in enumerate(masks)
        ]

        def pair_term(j, tests, lo=0, size=chunk):
            rows = both[j][:, :, lo:lo + size]
            return jnp.einsum("rsk,rtk->st", rows, tests, preferred_element_type=jnp.float32)

        along_x = lax.ppermute(mine, "rows", xor_pairs(owners_n, bx))
        along_y = lax.ppermute(mine, "rows", xor_pairs(owners_n, by))
        half = chunk // 2
        first = lax.ppermute(along_y[:, :, :half], "rows", xor_pairs(owners_n, bx))
        second = lax.ppermute(along_x[:, :, half:], "rows", xor_pairs(owners_n, by))
        paired = pair_term(0, mine) + pair_term(1, along_x) + pair_term(2, along_y)
        paired = paired + pair_term(3, first, 0, half) + pair_term(3, second, half, half)
        returned = lax.ppermute(paired[local_rows:], "rows", xor_pairs(owners_n, 1))
        remote = paired[:local_rows] + returned
    else:
        remote = term(here * chunk, chunk, mine)
        held = mine[None]
        masks = [0]
        for mask in chip_bits + [1]:
            got = lax.ppermute(held, "rows", xor_pairs(owners_n, mask))
            for j, m in enumerate(masks):
                remote = remote + term((here ^ mask ^ m) * chunk, chunk, got[j])
            held = jnp.concatenate([held, got], axis=0)
            masks = masks + [m ^ mask for m in masks]
    relative = jnp.concatenate([own, remote], axis=1)
    doubled = jnp.concatenate([relative, relative], axis=1)
    start = ((blocks_n - block) % blocks_n) * width
    total = lax.dynamic_slice_in_dim(doubled, start, blocks_n * width, axis=1)
    row_scores = total.astype(jnp.bfloat16)
    placed = jnp.dot(
        slot_matrix(owner_ids, owners_n, capacity), row_scores, preferred_element_type=jnp.float32
    ).astype(jnp.bfloat16)
    return lax.all_to_all(placed, "rows", split_axis=0, concat_axis=0, tiled=True)


def solution(mesh):
    return jax.shard_map(
        on_device,
        mesh=mesh,
        in_specs=(P(None, ("blk", "rows"), None), P(("blk", "rows"), None), P(None, "blk", None)),
        out_specs=P(("blk", "rows"), None),
        check_vma=False,
    )
```

```python
import jax
import jax.numpy as jnp
from jax import lax
from jax.sharding import PartitionSpec as P


def slot_matrix(owner_ids, owners_n, capacity):
    owner = owner_ids[:, 0]
    onehot = (owner[:, None] == jnp.arange(owners_n, dtype=jnp.int32)[None, :]).astype(jnp.int32)
    before = jnp.cumsum(onehot, axis=0) - onehot
    rank = jnp.sum(before * onehot, axis=1)
    slot = owner * capacity + rank
    slots = jnp.arange(owners_n * capacity, dtype=jnp.int32)
    return (slots[:, None] == slot[None, :]).astype(jnp.bfloat16)


def xor_pairs(count, mask):
    return [(s, s ^ mask) for s in range(count)]


def on_device(features, owner_ids, test_blocks):
    owners_n = lax.axis_size("rows")
    blocks_n = lax.axis_size("blk")
    local_rows = features.shape[1]
    width = test_blocks.shape[1]
    capacity = 2 * local_rows // owners_n
    chunk = features.shape[2] // owners_n
    here = lax.axis_index("rows")
    block = lax.axis_index("blk")

    def term(offset, size, tests):
        part = lax.dynamic_slice_in_dim(features, offset, size, axis=2)
        return jnp.einsum("rsk,rtk->st", part, tests, preferred_element_type=jnp.float32)

    piece = lax.dynamic_slice_in_dim(test_blocks, here * chunk, chunk, axis=2)
    arrived = []
    for step in range(1, blocks_n):
        pairs = [(b, (b - step) % blocks_n) for b in range(blocks_n)]
        arrived.append(lax.ppermute(piece, "blk", pairs))
    mine = jnp.concatenate(arrived, axis=1)
    own = jnp.einsum("rsk,rtk->st", features, test_blocks, preferred_element_type=jnp.float32)
    chip_bits = [1 << i for i in range(1, owners_n.bit_length() - 1)]
    if len(chip_bits) == 2:
        bx, by = chip_bits
        masks = [0, bx, by, bx ^ by]
        lent = jnp.stack(
            [lax.dynamic_slice_in_dim(features, (here ^ 1 ^ m) * chunk, chunk, axis=2) for m in masks]
        )
        mine, own, lent = lax.optimization_barrier((mine, own, lent))
        lent = lax.ppermute(lent, "rows", xor_pairs(owners_n, 1))
        both = [
            jnp.concatenate(
                [lax.dynamic_slice_in_dim(features, (here ^ m) * chunk, chunk, axis=2), lent[j]], axis=1
            )
            for j, m in enumerate(masks)
        ]

        def pair_term(j, tests, lo=0, size=None):
            rows = both[j][lo:lo + (size or both[j].shape[0])]
            return jnp.einsum("rsk,rtk->st", rows, tests, preferred_element_type=jnp.float32)

        along_x = lax.ppermute(mine, "rows", xor_pairs(owners_n, bx))
        along_y = lax.ppermute(mine, "rows", xor_pairs(owners_n, by))
        half = features.shape[0] // 2
        first = lax.ppermute(along_y[:half], "rows", xor_pairs(owners_n, bx))
        second = lax.ppermute(along_x[half:], "rows", xor_pairs(owners_n, by))
        paired = pair_term(0, mine) + pair_term(1, along_x) + pair_term(2, along_y)
        paired = paired + pair_term(3, first, 0, half) + pair_term(3, second, half, features.shape[0] - half)
        returned = lax.ppermute(paired[local_rows:], "rows", xor_pairs(owners_n, 1))
        remote = paired[:local_rows] + returned
    else:
        mine, own = lax.optimization_barrier((mine, own))
        remote = term(here * chunk, chunk, mine)
        held = mine[None]
        masks = [0]
        for mask in chip_bits + [1]:
            got = lax.ppermute(held, "rows", xor_pairs(owners_n, mask))
            for j, m in enumerate(masks):
                remote = remote + term((here ^ mask ^ m) * chunk, chunk, got[j])
            held = jnp.concatenate([held, got], axis=0)
            masks = masks + [m ^ mask for m in masks]
    relative = jnp.concatenate([own, remote], axis=1)
    doubled = jnp.concatenate([relative, relative], axis=1)
    start = ((blocks_n - block) % blocks_n) * width
    total = lax.dynamic_slice_in_dim(doubled, start, blocks_n * width, axis=1)
    row_scores = total.astype(jnp.bfloat16)
    placed = jnp.dot(
        slot_matrix(owner_ids, owners_n, capacity), row_scores, preferred_element_type=jnp.float32
    ).astype(jnp.bfloat16)
    return lax.all_to_all(placed, "rows", split_axis=0, concat_axis=0, tiled=True)


def solution(mesh):
    return jax.shard_map(
        on_device,
        mesh=mesh,
        in_specs=(P(None, ("blk", "rows"), None), P(("blk", "rows"), None), P(None, "blk", None)),
        out_specs=P(("blk", "rows"), None),
        check_vma=False,
    )
```

```python
import jax
import jax.numpy as jnp
from jax import lax
from jax.sharding import PartitionSpec as P


def slot_matrix(owner_ids, owners_n, capacity):
    owner = owner_ids[:, 0]
    onehot = (owner[:, None] == jnp.arange(owners_n, dtype=jnp.int32)[None, :]).astype(jnp.int32)
    before = jnp.cumsum(onehot, axis=0) - onehot
    rank = jnp.sum(before * onehot, axis=1)
    slot = owner * capacity + rank
    slots = jnp.arange(owners_n * capacity, dtype=jnp.int32)
    return (slots[:, None] == slot[None, :]).astype(jnp.bfloat16)


def xor_pairs(count, mask):
    return [(s, s ^ mask) for s in range(count)]


def on_device(features, owner_ids, test_blocks):
    owners_n = lax.axis_size("rows")
    blocks_n = lax.axis_size("blk")
    local_rows = features.shape[1]
    width = test_blocks.shape[1]
    capacity = 2 * local_rows // owners_n
    chunk = features.shape[2] // owners_n
    here = lax.axis_index("rows")
    block = lax.axis_index("blk")

    def term(offset, size, tests):
        part = lax.dynamic_slice_in_dim(features, offset, size, axis=2)
        return jnp.einsum("rsk,rtk->st", part, tests, preferred_element_type=jnp.float32)

    piece = lax.dynamic_slice_in_dim(test_blocks, here * chunk, chunk, axis=2)
    arrived = []
    for step in range(1, blocks_n):
        pairs = [(b, (b - step) % blocks_n) for b in range(blocks_n)]
        arrived.append(lax.ppermute(piece, "blk", pairs))
    mine = jnp.concatenate(arrived, axis=1)
    own = jnp.einsum("rsk,rtk->st", features, test_blocks, preferred_element_type=jnp.float32)
    slotting = slot_matrix(owner_ids, owners_n, capacity)
    mine, own, slotting = lax.optimization_barrier((mine, own, slotting))
    remote = term(here * chunk, chunk, mine)
    chip_bits = [1 << i for i in range(1, owners_n.bit_length() - 1)]
    if len(chip_bits) == 2:
        bx, by = chip_bits
        along_x = lax.ppermute(mine, "rows", xor_pairs(owners_n, bx))
        along_y = lax.ppermute(mine, "rows", xor_pairs(owners_n, by))
        remote = remote + term((here ^ bx) * chunk, chunk, along_x)
        remote = remote + term((here ^ by) * chunk, chunk, along_y)
        half = chunk // 2
        first = lax.ppermute(along_y[:, :, :half], "rows", xor_pairs(owners_n, bx))
        second = lax.ppermute(along_x[:, :, half:], "rows", xor_pairs(owners_n, by))
        corner = (here ^ bx ^ by) * chunk
        remote = remote + term(corner, half, first) + term(corner + half, half, second)
        diagonal = jnp.concatenate([first, second], axis=2)
        held = jnp.stack([mine, along_x, along_y, diagonal])
        masks = [0, bx, by, bx ^ by]
    else:
        held = mine[None]
        masks = [0]
        for mask in chip_bits:
            got = lax.ppermute(held, "rows", xor_pairs(owners_n, mask))
            for j, m in enumerate(masks):
                remote = remote + term((here ^ mask ^ m) * chunk, chunk, got[j])
            held = jnp.concatenate([held, got], axis=0)
            masks = masks + [m ^ mask for m in masks]
    if owners_n > 1:
        got = lax.ppermute(held, "rows", xor_pairs(owners_n, 1))
        for j, m in enumerate(masks):
            remote = remote + term((here ^ 1 ^ m) * chunk, chunk, got[j])
    relative = jnp.concatenate([own, remote], axis=1)
    doubled = jnp.concatenate([relative, relative], axis=1)
    start = ((blocks_n - block) % blocks_n) * width
    total = lax.dynamic_slice_in_dim(doubled, start, blocks_n * width, axis=1)
    row_scores = total.astype(jnp.bfloat16)
    placed = jnp.dot(
        slotting, row_scores, preferred_element_type=jnp.float32
    ).astype(jnp.bfloat16)
    return lax.all_to_all(placed, "rows", split_axis=0, concat_axis=0, tiled=True)


def solution(mesh):
    return jax.shard_map(
        on_device,
        mesh=mesh,
        in_specs=(P(None, ("blk", "rows"), None), P(("blk", "rows"), None), P(None, "blk", None)),
        out_specs=P(("blk", "rows"), None),
        check_vma=False,
    )
```

```python
import jax
import jax.numpy as jnp
from jax import lax
from jax.sharding import PartitionSpec as P


def slot_matrix(owner_ids, owners_n, capacity):
    owner = owner_ids[:, 0]
    onehot = (owner[:, None] == jnp.arange(owners_n, dtype=jnp.int32)[None, :]).astype(jnp.int32)
    before = jnp.cumsum(onehot, axis=0) - onehot
    rank = jnp.sum(before * onehot, axis=1)
    slot = owner * capacity + rank
    slots = jnp.arange(owners_n * capacity, dtype=jnp.int32)
    return (slots[:, None] == slot[None, :]).astype(jnp.bfloat16)


def xor_pairs(count, mask):
    return [(s, s ^ mask) for s in range(count)]


def on_device(features, owner_ids, test_blocks):
    owners_n = lax.axis_size("rows")
    blocks_n = lax.axis_size("blk")
    local_rows = features.shape[1]
    width = test_blocks.shape[1]
    capacity = 2 * local_rows // owners_n
    chunk = features.shape[2] // owners_n
    here = lax.axis_index("rows")
    block = lax.axis_index("blk")

    def term(offset, size, tests):
        part = lax.dynamic_slice_in_dim(features, offset, size, axis=2)
        return jnp.einsum("rsk,rtk->st", part, tests, preferred_element_type=jnp.float32)

    piece = lax.dynamic_slice_in_dim(test_blocks, here * chunk, chunk, axis=2)
    arrived = []
    for step in range(1, blocks_n):
        pairs = [(b, (b - step) % blocks_n) for b in range(blocks_n)]
        arrived.append(lax.ppermute(piece, "blk", pairs))
    mine = jnp.concatenate(arrived, axis=1)
    own = jnp.einsum("rsk,rtk->st", features, test_blocks, preferred_element_type=jnp.float32)
    slotting = slot_matrix(owner_ids, owners_n, capacity)
    mine, own, slotting = lax.optimization_barrier((mine, own, slotting))
    remote = term(here * chunk, chunk, mine)
    chip_bits = [1 << i for i in range(1, owners_n.bit_length() - 1)]
    if len(chip_bits) == 2:
        bx, by = chip_bits
        along_x = lax.ppermute(mine, "rows", xor_pairs(owners_n, bx))
        along_y = lax.ppermute(mine, "rows", xor_pairs(owners_n, by))
        remote = remote + term((here ^ bx) * chunk, chunk, along_x)
        remote = remote + term((here ^ by) * chunk, chunk, along_y)
        half = chunk // 2
        first = lax.ppermute(along_y[:, :, :half], "rows", xor_pairs(owners_n, bx))
        second = lax.ppermute(along_x[:, :, half:], "rows", xor_pairs(owners_n, by))
        corner = (here ^ bx ^ by) * chunk
        remote = remote + term(corner, half, first) + term(corner + half, half, second)
        sibling = xor_pairs(owners_n, 1)
        for mask, got in ((0, mine), (bx, along_x), (by, along_y)):
            remote = remote + term((here ^ 1 ^ mask) * chunk, chunk, lax.ppermute(got, "rows", sibling))
        far = (here ^ 1 ^ bx ^ by) * chunk
        remote = remote + term(far, half, lax.ppermute(first, "rows", sibling))
        remote = remote + term(far + half, half, lax.ppermute(second, "rows", sibling))
    else:
        held = mine[None]
        masks = [0]
        for mask in chip_bits:
            got = lax.ppermute(held, "rows", xor_pairs(owners_n, mask))
            for j, m in enumerate(masks):
                remote = remote + term((here ^ mask ^ m) * chunk, chunk, got[j])
            held = jnp.concatenate([held, got], axis=0)
            masks = masks + [m ^ mask for m in masks]
        if owners_n > 1:
            got = lax.ppermute(held, "rows", xor_pairs(owners_n, 1))
            for j, m in enumerate(masks):
                remote = remote + term((here ^ 1 ^ m) * chunk, chunk, got[j])
    relative = jnp.concatenate([own, remote], axis=1)
    doubled = jnp.concatenate([relative, relative], axis=1)
    start = ((blocks_n - block) % blocks_n) * width
    total = lax.dynamic_slice_in_dim(doubled, start, blocks_n * width, axis=1)
    row_scores = total.astype(jnp.bfloat16)
    placed = jnp.dot(
        slotting, row_scores, preferred_element_type=jnp.float32
    ).astype(jnp.bfloat16)
    return lax.all_to_all(placed, "rows", split_axis=0, concat_axis=0, tiled=True)


def solution(mesh):
    return jax.shard_map(
        on_device,
        mesh=mesh,
        in_specs=(P(None, ("blk", "rows"), None), P(("blk", "rows"), None), P(None, "blk", None)),
        out_specs=P(("blk", "rows"), None),
        check_vma=False,
    )
```

```python
import jax
import jax.numpy as jnp
from jax import lax
from jax.sharding import PartitionSpec as P


def slot_matrix(owner_ids, owners_n, capacity):
    owner = owner_ids[:, 0]
    onehot = (owner[:, None] == jnp.arange(owners_n, dtype=jnp.int32)[None, :]).astype(jnp.int32)
    before = jnp.cumsum(onehot, axis=0) - onehot
    rank = jnp.sum(before * onehot, axis=1)
    slot = owner * capacity + rank
    slots = jnp.arange(owners_n * capacity, dtype=jnp.int32)
    return (slots[:, None] == slot[None, :]).astype(jnp.bfloat16)


def xor_pairs(count, mask):
    return [(s, s ^ mask) for s in range(count)]


def on_device(features, owner_ids, test_blocks):
    owners_n = lax.axis_size("rows")
    blocks_n = lax.axis_size("blk")
    local_rows = features.shape[1]
    width = test_blocks.shape[1]
    capacity = 2 * local_rows // owners_n
    chunk = features.shape[2] // owners_n
    here = lax.axis_index("rows")
    block = lax.axis_index("blk")

    def term(offset, size, tests):
        part = lax.dynamic_slice_in_dim(features, offset, size, axis=2)
        return jnp.einsum("rsk,rtk->st", part, tests, preferred_element_type=jnp.float32)

    piece = lax.dynamic_slice_in_dim(test_blocks, here * chunk, chunk, axis=2)
    arrived = []
    for step in range(1, blocks_n):
        pairs = [(b, (b - step) % blocks_n) for b in range(blocks_n)]
        arrived.append(lax.ppermute(piece, "blk", pairs))
    mine = jnp.concatenate(arrived, axis=1)
    own = jnp.einsum("rsk,rtk->st", features, test_blocks, preferred_element_type=jnp.float32)
    slotting = slot_matrix(owner_ids, owners_n, capacity)
    mine, own, slotting = lax.optimization_barrier((mine, own, slotting))
    remote = term(here * chunk, chunk, mine)
    chip_bits = [1 << i for i in range(1, owners_n.bit_length() - 1)]
    if len(chip_bits) == 2:
        bx, by = chip_bits
        along_x = lax.ppermute(mine, "rows", xor_pairs(owners_n, bx))
        along_y = lax.ppermute(mine, "rows", xor_pairs(owners_n, by))
        remote = remote + term((here ^ bx) * chunk, chunk, along_x)
        remote = remote + term((here ^ by) * chunk, chunk, along_y)
        across = lax.ppermute(mine, "rows", xor_pairs(owners_n, bx ^ by))
        remote = remote + term((here ^ bx ^ by) * chunk, chunk, across)
        sibling = xor_pairs(owners_n, 1)
        for mask, got in ((0, mine), (bx, along_x), (by, along_y), (bx ^ by, across)):
            remote = remote + term((here ^ 1 ^ mask) * chunk, chunk, lax.ppermute(got, "rows", sibling))
    else:
        held = mine[None]
        masks = [0]
        for mask in chip_bits:
            got = lax.ppermute(held, "rows", xor_pairs(owners_n, mask))
            for j, m in enumerate(masks):
                remote = remote + term((here ^ mask ^ m) * chunk, chunk, got[j])
            held = jnp.concatenate([held, got], axis=0)
            masks = masks + [m ^ mask for m in masks]
        if owners_n > 1:
            got = lax.ppermute(held, "rows", xor_pairs(owners_n, 1))
            for j, m in enumerate(masks):
                remote = remote + term((here ^ 1 ^ m) * chunk, chunk, got[j])
    relative = jnp.concatenate([own, remote], axis=1)
    doubled = jnp.concatenate([relative, relative], axis=1)
    start = ((blocks_n - block) % blocks_n) * width
    total = lax.dynamic_slice_in_dim(doubled, start, blocks_n * width, axis=1)
    row_scores = total.astype(jnp.bfloat16)
    placed = jnp.dot(
        slotting, row_scores, preferred_element_type=jnp.float32
    ).astype(jnp.bfloat16)
    return lax.all_to_all(placed, "rows", split_axis=0, concat_axis=0, tiled=True)


def solution(mesh):
    return jax.shard_map(
        on_device,
        mesh=mesh,
        in_specs=(P(None, ("blk", "rows"), None), P(("blk", "rows"), None), P(None, "blk", None)),
        out_specs=P(("blk", "rows"), None),
        check_vma=False,
    )
```

```python
import jax
import jax.numpy as jnp
from jax import lax
from jax.sharding import PartitionSpec as P


def slot_matrix(owner_ids, owners_n, capacity):
    owner = owner_ids[:, 0]
    onehot = (owner[:, None] == jnp.arange(owners_n, dtype=jnp.int32)[None, :]).astype(jnp.int32)
    before = jnp.cumsum(onehot, axis=0) - onehot
    rank = jnp.sum(before * onehot, axis=1)
    slot = owner * capacity + rank
    slots = jnp.arange(owners_n * capacity, dtype=jnp.int32)
    return (slots[:, None] == slot[None, :]).astype(jnp.bfloat16)


def xor_pairs(count, mask):
    return [(s, s ^ mask) for s in range(count)]


def on_device(features, owner_ids, test_blocks):
    owners_n = lax.axis_size("rows")
    blocks_n = lax.axis_size("blk")
    local_rows = features.shape[1]
    width = test_blocks.shape[1]
    capacity = 2 * local_rows // owners_n
    chunk = features.shape[2] // owners_n
    here = lax.axis_index("rows")
    block = lax.axis_index("blk")

    def term(offset, size, tests):
        part = lax.dynamic_slice_in_dim(features, offset, size, axis=2)
        return jnp.einsum("rsk,rtk->st", part, tests, preferred_element_type=jnp.float32)

    piece = test_blocks[:, :, :chunk]
    for c in range(1, owners_n):
        piece = jnp.where(here == c, test_blocks[:, :, c * chunk:(c + 1) * chunk], piece)
    arrived = []
    for step in range(1, blocks_n):
        pairs = [(b, (b - step) % blocks_n) for b in range(blocks_n)]
        arrived.append(lax.ppermute(piece, "blk", pairs))
    mine = jnp.concatenate(arrived, axis=1)
    own = jnp.einsum("rsk,rtk->st", features, test_blocks, preferred_element_type=jnp.float32)
    slotting = slot_matrix(owner_ids, owners_n, capacity)
    mine, own, slotting = lax.optimization_barrier((mine, own, slotting))
    remote = term(here * chunk, chunk, mine)
    chip_bits = [1 << i for i in range(1, owners_n.bit_length() - 1)]
    if len(chip_bits) == 2:
        bx, by = chip_bits
        along_x = lax.ppermute(mine, "rows", xor_pairs(owners_n, bx))
        along_y = lax.ppermute(mine, "rows", xor_pairs(owners_n, by))
        remote = remote + term((here ^ bx) * chunk, chunk, along_x)
        remote = remote + term((here ^ by) * chunk, chunk, along_y)
        half = chunk // 2
        first = lax.ppermute(along_y[:, :, :half], "rows", xor_pairs(owners_n, bx))
        second = lax.ppermute(along_x[:, :, half:], "rows", xor_pairs(owners_n, by))
        corner = (here ^ bx ^ by) * chunk
        remote = remote + term(corner, half, first) + term(corner + half, half, second)
        sibling = xor_pairs(owners_n, 1)
        for mask, got in ((0, mine), (bx, along_x), (by, along_y)):
            remote = remote + term((here ^ 1 ^ mask) * chunk, chunk, lax.ppermute(got, "rows", sibling))
        far = (here ^ 1 ^ bx ^ by) * chunk
        remote = remote + term(far, half, lax.ppermute(first, "rows", sibling))
        remote = remote + term(far + half, half, lax.ppermute(second, "rows", sibling))
    else:
        held = mine[None]
        masks = [0]
        for mask in chip_bits:
            got = lax.ppermute(held, "rows", xor_pairs(owners_n, mask))
            for j, m in enumerate(masks):
                remote = remote + term((here ^ mask ^ m) * chunk, chunk, got[j])
            held = jnp.concatenate([held, got], axis=0)
            masks = masks + [m ^ mask for m in masks]
        if owners_n > 1:
            got = lax.ppermute(held, "rows", xor_pairs(owners_n, 1))
            for j, m in enumerate(masks):
                remote = remote + term((here ^ 1 ^ m) * chunk, chunk, got[j])
    relative = jnp.concatenate([own, remote], axis=1)
    doubled = jnp.concatenate([relative, relative], axis=1)
    start = ((blocks_n - block) % blocks_n) * width
    total = lax.dynamic_slice_in_dim(doubled, start, blocks_n * width, axis=1)
    row_scores = total.astype(jnp.bfloat16)
    placed = jnp.dot(
        slotting, row_scores, preferred_element_type=jnp.float32
    ).astype(jnp.bfloat16)
    return lax.all_to_all(placed, "rows", split_axis=0, concat_axis=0, tiled=True)


def solution(mesh):
    return jax.shard_map(
        on_device,
        mesh=mesh,
        in_specs=(P(None, ("blk", "rows"), None), P(("blk", "rows"), None), P(None, "blk", None)),
        out_specs=P(("blk", "rows"), None),
        check_vma=False,
    )
```

```python
import jax
import jax.numpy as jnp
from jax import lax
from jax.sharding import PartitionSpec as P


def slot_matrix(owner_ids, owners_n, capacity):
    owner = owner_ids[:, 0]
    onehot = (owner[:, None] == jnp.arange(owners_n, dtype=jnp.int32)[None, :]).astype(jnp.int32)
    before = jnp.cumsum(onehot, axis=0) - onehot
    rank = jnp.sum(before * onehot, axis=1)
    slot = owner * capacity + rank
    slots = jnp.arange(owners_n * capacity, dtype=jnp.int32)
    return (slots[:, None] == slot[None, :]).astype(jnp.bfloat16)


def xor_pairs(count, mask):
    return [(s, s ^ mask) for s in range(count)]


def on_device(features, owner_ids, test_blocks):
    owners_n = lax.axis_size("rows")
    blocks_n = lax.axis_size("blk")
    runs = features.shape[0]
    local_rows = features.shape[1]
    width = test_blocks.shape[1]
    capacity = 2 * local_rows // owners_n
    chunk = features.shape[2] // owners_n
    here = lax.axis_index("rows")
    block = lax.axis_index("blk")

    def term(offset, size, tests):
        part = lax.dynamic_slice_in_dim(features, offset, size, axis=2)
        return jnp.einsum("rsk,rtk->st", part, tests, preferred_element_type=jnp.float32)

    chip_bits = [1 << i for i in range(1, owners_n.bit_length() - 1)]
    split_runs = len(chip_bits) == 2 and runs % 2 == 0
    if split_runs:
        span = runs // 2
        quarter = features.shape[2] // (owners_n // 2)
        core = here % 2
        chip = here // 2
        piece = lax.dynamic_slice(test_blocks, (core * span, 0, chip * quarter), (span, width, quarter))
        lent = lax.dynamic_slice_in_dim(features, (1 - core) * span, span, axis=0)
    else:
        piece = lax.dynamic_slice_in_dim(test_blocks, here * chunk, chunk, axis=2)
    arrived = []
    for step in range(1, blocks_n):
        pairs = [(b, (b - step) % blocks_n) for b in range(blocks_n)]
        arrived.append(lax.ppermute(piece, "blk", pairs))
    mine = jnp.concatenate(arrived, axis=1)
    own = jnp.einsum("rsk,rtk->st", features, test_blocks, preferred_element_type=jnp.float32)
    slotting = slot_matrix(owner_ids, owners_n, capacity)
    if split_runs:
        bx, by = chip_bits
        lent = lax.ppermute(lent, "rows", xor_pairs(owners_n, 1))
        mine, own, slotting = lax.optimization_barrier((mine, own, slotting))
        rows_all = jnp.concatenate([lax.dynamic_slice_in_dim(features, core * span, span, axis=0), lent], axis=1)

        def pair_term(chip_of, tests, lo=0, size=quarter):
            part = lax.dynamic_slice_in_dim(rows_all, chip_of * quarter + lo, size, axis=2)
            return jnp.einsum("rsk,rtk->st", part, tests, preferred_element_type=jnp.float32)

        along_x = lax.ppermute(mine, "rows", xor_pairs(owners_n, bx))
        along_y = lax.ppermute(mine, "rows", xor_pairs(owners_n, by))
        half = quarter // 2
        first = lax.ppermute(along_y[:, :, :half], "rows", xor_pairs(owners_n, bx))
        second = lax.ppermute(along_x[:, :, half:], "rows", xor_pairs(owners_n, by))
        paired = pair_term(chip, mine) + pair_term(chip ^ (bx // 2), along_x) + pair_term(chip ^ (by // 2), along_y)
        corner = chip ^ ((bx ^ by) // 2)
        paired = paired + pair_term(corner, first, 0, half) + pair_term(corner, second, half, half)
        returned = lax.ppermute(paired[local_rows:], "rows", xor_pairs(owners_n, 1))
        remote = paired[:local_rows] + returned
    else:
        mine, own, slotting = lax.optimization_barrier((mine, own, slotting))
        remote = term(here * chunk, chunk, mine)
        held = mine[None]
        masks = [0]
        for mask in chip_bits + [1]:
            got = lax.ppermute(held, "rows", xor_pairs(owners_n, mask))
            for j, m in enumerate(masks):
                remote = remote + term((here ^ mask ^ m) * chunk, chunk, got[j])
            held = jnp.concatenate([held, got], axis=0)
            masks = masks + [m ^ mask for m in masks]
    relative = jnp.concatenate([own, remote], axis=1)
    doubled = jnp.concatenate([relative, relative], axis=1)
    start = ((blocks_n - block) % blocks_n) * width
    total = lax.dynamic_slice_in_dim(doubled, start, blocks_n * width, axis=1)
    row_scores = total.astype(jnp.bfloat16)
    placed = jnp.dot(
        slotting, row_scores, preferred_element_type=jnp.float32
    ).astype(jnp.bfloat16)
    return lax.all_to_all(placed, "rows", split_axis=0, concat_axis=0, tiled=True)


def solution(mesh):
    return jax.shard_map(
        on_device,
        mesh=mesh,
        in_specs=(P(None, ("blk", "rows"), None), P(("blk", "rows"), None), P(None, "blk", None)),
        out_specs=P(("blk", "rows"), None),
        check_vma=False,
    )
```

```python
import jax
import jax.numpy as jnp
from jax import lax
from jax.sharding import PartitionSpec as P


def slot_matrix(owner_ids, owners_n, capacity):
    owner = owner_ids[:, 0]
    onehot = (owner[:, None] == jnp.arange(owners_n, dtype=jnp.int32)[None, :]).astype(jnp.int32)
    before = jnp.cumsum(onehot, axis=0) - onehot
    rank = jnp.sum(before * onehot, axis=1)
    slot = owner * capacity + rank
    slots = jnp.arange(owners_n * capacity, dtype=jnp.int32)
    return (slots[:, None] == slot[None, :]).astype(jnp.bfloat16)


def xor_pairs(count, mask):
    return [(s, s ^ mask) for s in range(count)]


def on_device(features, owner_ids, test_blocks):
    owners_n = lax.axis_size("rows")
    blocks_n = lax.axis_size("blk")
    local_rows = features.shape[1]
    width = test_blocks.shape[1]
    capacity = 2 * local_rows // owners_n
    chunk = features.shape[2] // owners_n
    here = lax.axis_index("rows")
    block = lax.axis_index("blk")

    def term(offset, size, tests):
        part = lax.dynamic_slice_in_dim(features, offset, size, axis=2)
        return jnp.einsum("rsk,rtk->st", part, tests, preferred_element_type=jnp.float32)

    piece = lax.dynamic_slice_in_dim(test_blocks, here * chunk, chunk, axis=2)
    arrived = []
    for step in range(1, blocks_n):
        pairs = [(b, (b - step) % blocks_n) for b in range(blocks_n)]
        arrived.append(lax.ppermute(piece, "blk", pairs))
    mine = jnp.concatenate(arrived, axis=1)
    own = jnp.einsum("rsk,rtk->st", features, test_blocks, preferred_element_type=jnp.float32)
    slotting = slot_matrix(owner_ids, owners_n, capacity)
    mine, own, slotting = lax.optimization_barrier((mine, own, slotting))
    remote = term(here * chunk, chunk, mine)
    chip_bits = [1 << i for i in range(1, owners_n.bit_length() - 1)]
    if len(chip_bits) == 2:
        bx, by = chip_bits
        along_x = lax.ppermute(mine, "rows", xor_pairs(owners_n, bx))
        along_y = lax.ppermute(mine, "rows", xor_pairs(owners_n, by))
        mine, along_x, along_y = lax.optimization_barrier((mine, along_x, along_y))
        remote = remote + term((here ^ bx) * chunk, chunk, along_x)
        remote = remote + term((here ^ by) * chunk, chunk, along_y)
        half = chunk // 2
        first = lax.ppermute(along_y[:, :, :half], "rows", xor_pairs(owners_n, bx))
        second = lax.ppermute(along_x[:, :, half:], "rows", xor_pairs(owners_n, by))
        corner = (here ^ bx ^ by) * chunk
        remote = remote + term(corner, half, first) + term(corner + half, half, second)
        sibling = xor_pairs(owners_n, 1)
        for mask, got in ((0, mine), (bx, along_x), (by, along_y)):
            remote = remote + term((here ^ 1 ^ mask) * chunk, chunk, lax.ppermute(got, "rows", sibling))
        far = (here ^ 1 ^ bx ^ by) * chunk
        remote = remote + term(far, half, lax.ppermute(first, "rows", sibling))
        remote = remote + term(far + half, half, lax.ppermute(second, "rows", sibling))
    else:
        held = mine[None]
        masks = [0]
        for mask in chip_bits:
            got = lax.ppermute(held, "rows", xor_pairs(owners_n, mask))
            for j, m in enumerate(masks):
                remote = remote + term((here ^ mask ^ m) * chunk, chunk, got[j])
            held = jnp.concatenate([held, got], axis=0)
            masks = masks + [m ^ mask for m in masks]
        if owners_n > 1:
            got = lax.ppermute(held, "rows", xor_pairs(owners_n, 1))
            for j, m in enumerate(masks):
                remote = remote + term((here ^ 1 ^ m) * chunk, chunk, got[j])
    relative = jnp.concatenate([own, remote], axis=1)
    doubled = jnp.concatenate([relative, relative], axis=1)
    start = ((blocks_n - block) % blocks_n) * width
    total = lax.dynamic_slice_in_dim(doubled, start, blocks_n * width, axis=1)
    row_scores = total.astype(jnp.bfloat16)
    placed = jnp.dot(
        slotting, row_scores, preferred_element_type=jnp.float32
    ).astype(jnp.bfloat16)
    return lax.all_to_all(placed, "rows", split_axis=0, concat_axis=0, tiled=True)


def solution(mesh):
    return jax.shard_map(
        on_device,
        mesh=mesh,
        in_specs=(P(None, ("blk", "rows"), None), P(("blk", "rows"), None), P(None, "blk", None)),
        out_specs=P(("blk", "rows"), None),
        check_vma=False,
    )
```

```python
import jax
import jax.numpy as jnp
from jax import lax
from jax.sharding import PartitionSpec as P


def slot_matrix(owner_ids, owners_n, capacity):
    owner = owner_ids[:, 0]
    onehot = (owner[:, None] == jnp.arange(owners_n, dtype=jnp.int32)[None, :]).astype(jnp.int32)
    before = jnp.cumsum(onehot, axis=0) - onehot
    rank = jnp.sum(before * onehot, axis=1)
    slot = owner * capacity + rank
    slots = jnp.arange(owners_n * capacity, dtype=jnp.int32)
    return (slots[:, None] == slot[None, :]).astype(jnp.bfloat16)


def xor_pairs(count, mask):
    return [(s, s ^ mask) for s in range(count)]


def on_device(features, owner_ids, test_blocks):
    owners_n = lax.axis_size("rows")
    blocks_n = lax.axis_size("blk")
    local_rows = features.shape[1]
    width = test_blocks.shape[1]
    capacity = 2 * local_rows // owners_n
    chunk = features.shape[2] // owners_n
    here = lax.axis_index("rows")
    block = lax.axis_index("blk")

    def term(offset, size, tests):
        part = lax.dynamic_slice_in_dim(features, offset, size, axis=2)
        return jnp.einsum("rsk,rtk->st", part, tests, preferred_element_type=jnp.float32)

    piece = lax.dynamic_slice_in_dim(test_blocks, here * chunk, chunk, axis=2)
    arrived = []
    for step in range(1, blocks_n):
        pairs = [(b, (b - step) % blocks_n) for b in range(blocks_n)]
        arrived.append(lax.ppermute(piece, "blk", pairs))
    mine = jnp.concatenate(arrived, axis=1)
    own = jnp.einsum("rsk,rtk->st", features, test_blocks, preferred_element_type=jnp.float32)
    slotting = slot_matrix(owner_ids, owners_n, capacity)
    mine, own, slotting = lax.optimization_barrier((mine, own, slotting))
    remote = term(here * chunk, chunk, mine)
    chip_bits = [1 << i for i in range(1, owners_n.bit_length() - 1)]
    if len(chip_bits) == 2:
        bx, by = chip_bits
        along_x = lax.ppermute(mine, "rows", xor_pairs(owners_n, bx))
        along_y = lax.ppermute(mine, "rows", xor_pairs(owners_n, by))
        remote = remote + term((here ^ bx) * chunk, chunk, along_x)
        remote = remote + term((here ^ by) * chunk, chunk, along_y)
        sibling = xor_pairs(owners_n, 1)
        for mask, got in ((0, mine), (bx, along_x), (by, along_y)):
            remote = remote + term((here ^ 1 ^ mask) * chunk, chunk, lax.ppermute(got, "rows", sibling))
        half = chunk // 2
        first = lax.ppermute(along_y[:, :, :half], "rows", xor_pairs(owners_n, bx))
        second = lax.ppermute(along_x[:, :, half:], "rows", xor_pairs(owners_n, by))
        corner = (here ^ bx ^ by) * chunk
        remote = remote + term(corner, half, first) + term(corner + half, half, second)
        far = (here ^ 1 ^ bx ^ by) * chunk
        remote = remote + term(far, half, lax.ppermute(first, "rows", sibling))
        remote = remote + term(far + half, half, lax.ppermute(second, "rows", sibling))
    else:
        held = mine[None]
        masks = [0]
        for mask in chip_bits:
            got = lax.ppermute(held, "rows", xor_pairs(owners_n, mask))
            for j, m in enumerate(masks):
                remote = remote + term((here ^ mask ^ m) * chunk, chunk, got[j])
            held = jnp.concatenate([held, got], axis=0)
            masks = masks + [m ^ mask for m in masks]
        if owners_n > 1:
            got = lax.ppermute(held, "rows", xor_pairs(owners_n, 1))
            for j, m in enumerate(masks):
                remote = remote + term((here ^ 1 ^ m) * chunk, chunk, got[j])
    relative = jnp.concatenate([own, remote], axis=1)
    doubled = jnp.concatenate([relative, relative], axis=1)
    start = ((blocks_n - block) % blocks_n) * width
    total = lax.dynamic_slice_in_dim(doubled, start, blocks_n * width, axis=1)
    row_scores = total.astype(jnp.bfloat16)
    placed = jnp.dot(
        slotting, row_scores, preferred_element_type=jnp.float32
    ).astype(jnp.bfloat16)
    return lax.all_to_all(placed, "rows", split_axis=0, concat_axis=0, tiled=True)


def solution(mesh):
    return jax.shard_map(
        on_device,
        mesh=mesh,
        in_specs=(P(None, ("blk", "rows"), None), P(("blk", "rows"), None), P(None, "blk", None)),
        out_specs=P(("blk", "rows"), None),
        check_vma=False,
    )
```

```python
import jax
import jax.numpy as jnp
from jax import lax
from jax.sharding import PartitionSpec as P


def slot_matrix(owner_ids, owners_n, capacity):
    owner = owner_ids[:, 0]
    onehot = (owner[:, None] == jnp.arange(owners_n, dtype=jnp.int32)[None, :]).astype(jnp.int32)
    before = jnp.cumsum(onehot, axis=0) - onehot
    rank = jnp.sum(before * onehot, axis=1)
    slot = owner * capacity + rank
    slots = jnp.arange(owners_n * capacity, dtype=jnp.int32)
    return (slots[:, None] == slot[None, :]).astype(jnp.bfloat16)


def xor_pairs(count, mask):
    return [(s, s ^ mask) for s in range(count)]


def on_device(features, owner_ids, test_blocks):
    owners_n = lax.axis_size("rows")
    blocks_n = lax.axis_size("blk")
    local_rows = features.shape[1]
    width = test_blocks.shape[1]
    capacity = 2 * local_rows // owners_n
    chunk = features.shape[2] // owners_n
    here = lax.axis_index("rows")
    block = lax.axis_index("blk")

    def term(offset, size, tests):
        part = lax.dynamic_slice_in_dim(features, offset, size, axis=2)
        return jnp.einsum("rsk,rtk->st", part, tests, preferred_element_type=jnp.float32)

    piece = lax.dynamic_slice_in_dim(test_blocks, here * chunk, chunk, axis=2)
    arrived = []
    for step in range(1, blocks_n):
        pairs = [(b, (b - step) % blocks_n) for b in range(blocks_n)]
        arrived.append(lax.ppermute(piece, "blk", pairs))
    mine = jnp.concatenate(arrived, axis=1)
    own = jnp.einsum("rsk,rtk->st", features, test_blocks, preferred_element_type=jnp.float32)
    slotting = slot_matrix(owner_ids, owners_n, capacity)
    mine, own, slotting = lax.optimization_barrier((mine, own, slotting))
    remote = term(here * chunk, chunk, mine)
    chip_bits = [1 << i for i in range(1, owners_n.bit_length() - 1)]
    if len(chip_bits) == 2:
        bx, by = chip_bits
        along_x = lax.ppermute(mine, "rows", xor_pairs(owners_n, bx))
        along_y = lax.ppermute(mine, "rows", xor_pairs(owners_n, by))
        remote = remote + term((here ^ bx) * chunk, chunk, along_x)
        remote = remote + term((here ^ by) * chunk, chunk, along_y)
        relay = jnp.where(here % 2 == 0, along_y, along_x)
        pairs = [(s ^ (bx if s % 2 == 0 else by), s) for s in range(owners_n)]
        across = lax.ppermute(relay, "rows", pairs)
        remote = remote + term((here ^ bx ^ by) * chunk, chunk, across)
        sibling = xor_pairs(owners_n, 1)
        for mask, got in ((0, mine), (bx, along_x), (by, along_y), (bx ^ by, across)):
            remote = remote + term((here ^ 1 ^ mask) * chunk, chunk, lax.ppermute(got, "rows", sibling))
    else:
        held = mine[None]
        masks = [0]
        for mask in chip_bits:
            got = lax.ppermute(held, "rows", xor_pairs(owners_n, mask))
            for j, m in enumerate(masks):
                remote = remote + term((here ^ mask ^ m) * chunk, chunk, got[j])
            held = jnp.concatenate([held, got], axis=0)
            masks = masks + [m ^ mask for m in masks]
        if owners_n > 1:
            got = lax.ppermute(held, "rows", xor_pairs(owners_n, 1))
            for j, m in enumerate(masks):
                remote = remote + term((here ^ 1 ^ m) * chunk, chunk, got[j])
    relative = jnp.concatenate([own, remote], axis=1)
    doubled = jnp.concatenate([relative, relative], axis=1)
    start = ((blocks_n - block) % blocks_n) * width
    total = lax.dynamic_slice_in_dim(doubled, start, blocks_n * width, axis=1)
    row_scores = total.astype(jnp.bfloat16)
    placed = jnp.dot(
        slotting, row_scores, preferred_element_type=jnp.float32
    ).astype(jnp.bfloat16)
    return lax.all_to_all(placed, "rows", split_axis=0, concat_axis=0, tiled=True)


def solution(mesh):
    return jax.shard_map(
        on_device,
        mesh=mesh,
        in_specs=(P(None, ("blk", "rows"), None), P(("blk", "rows"), None), P(None, "blk", None)),
        out_specs=P(("blk", "rows"), None),
        check_vma=False,
    )
```

```python
import jax
import jax.numpy as jnp
from jax import lax
from jax.sharding import PartitionSpec as P


def slot_matrix(owner_ids, owners_n, capacity):
    owner = owner_ids[:, 0]
    onehot = (owner[:, None] == jnp.arange(owners_n, dtype=jnp.int32)[None, :]).astype(jnp.int32)
    before = jnp.cumsum(onehot, axis=0) - onehot
    rank = jnp.sum(before * onehot, axis=1)
    slot = owner * capacity + rank
    slots = jnp.arange(owners_n * capacity, dtype=jnp.int32)
    return (slots[:, None] == slot[None, :]).astype(jnp.bfloat16)


def xor_pairs(count, mask):
    return [(s, s ^ mask) for s in range(count)]


def on_device(features, owner_ids, test_blocks):
    owners_n = lax.axis_size("rows")
    blocks_n = lax.axis_size("blk")
    local_rows = features.shape[1]
    width = test_blocks.shape[1]
    capacity = 2 * local_rows // owners_n
    chunk = features.shape[2] // owners_n
    here = lax.axis_index("rows")
    block = lax.axis_index("blk")

    def term(offset, size, tests):
        part = lax.dynamic_slice_in_dim(features, offset, size, axis=2)
        return jnp.einsum("rsk,rtk->st", part, tests, preferred_element_type=jnp.float32)

    piece = lax.dynamic_slice_in_dim(test_blocks, here * chunk, chunk, axis=2)
    arrived = []
    for step in range(1, blocks_n):
        pairs = [(b, (b - step) % blocks_n) for b in range(blocks_n)]
        arrived.append(lax.ppermute(piece, "blk", pairs))
    mine = jnp.concatenate(arrived, axis=1)
    own = jnp.einsum("rsk,rtk->st", features, test_blocks, preferred_element_type=jnp.float32)
    slotting = slot_matrix(owner_ids, owners_n, capacity)
    mine, own, slotting = lax.optimization_barrier((mine, own, slotting))
    remote = term(here * chunk, chunk, mine)
    chip_bits = [1 << i for i in range(1, owners_n.bit_length() - 1)]
    if len(chip_bits) == 2:
        bx, by = chip_bits
        along_x = jnp.concatenate([lax.ppermute(a, "rows", xor_pairs(owners_n, bx)) for a in arrived], axis=1)
        along_y = jnp.concatenate([lax.ppermute(a, "rows", xor_pairs(owners_n, by)) for a in arrived], axis=1)
        remote = remote + term((here ^ bx) * chunk, chunk, along_x)
        remote = remote + term((here ^ by) * chunk, chunk, along_y)
        half = chunk // 2
        first = lax.ppermute(along_y[:, :, :half], "rows", xor_pairs(owners_n, bx))
        second = lax.ppermute(along_x[:, :, half:], "rows", xor_pairs(owners_n, by))
        corner = (here ^ bx ^ by) * chunk
        remote = remote + term(corner, half, first) + term(corner + half, half, second)
        sibling = xor_pairs(owners_n, 1)
        for mask, got in ((0, mine), (bx, along_x), (by, along_y)):
            remote = remote + term((here ^ 1 ^ mask) * chunk, chunk, lax.ppermute(got, "rows", sibling))
        far = (here ^ 1 ^ bx ^ by) * chunk
        remote = remote + term(far, half, lax.ppermute(first, "rows", sibling))
        remote = remote + term(far + half, half, lax.ppermute(second, "rows", sibling))
    else:
        held = mine[None]
        masks = [0]
        for mask in chip_bits:
            got = lax.ppermute(held, "rows", xor_pairs(owners_n, mask))
            for j, m in enumerate(masks):
                remote = remote + term((here ^ mask ^ m) * chunk, chunk, got[j])
            held = jnp.concatenate([held, got], axis=0)
            masks = masks + [m ^ mask for m in masks]
        if owners_n > 1:
            got = lax.ppermute(held, "rows", xor_pairs(owners_n, 1))
            for j, m in enumerate(masks):
                remote = remote + term((here ^ 1 ^ m) * chunk, chunk, got[j])
    relative = jnp.concatenate([own, remote], axis=1)
    doubled = jnp.concatenate([relative, relative], axis=1)
    start = ((blocks_n - block) % blocks_n) * width
    total = lax.dynamic_slice_in_dim(doubled, start, blocks_n * width, axis=1)
    row_scores = total.astype(jnp.bfloat16)
    placed = jnp.dot(
        slotting, row_scores, preferred_element_type=jnp.float32
    ).astype(jnp.bfloat16)
    return lax.all_to_all(placed, "rows", split_axis=0, concat_axis=0, tiled=True)


def solution(mesh):
    return jax.shard_map(
        on_device,
        mesh=mesh,
        in_specs=(P(None, ("blk", "rows"), None), P(("blk", "rows"), None), P(None, "blk", None)),
        out_specs=P(("blk", "rows"), None),
        check_vma=False,
    )
```

```python
import jax
import jax.numpy as jnp
from jax import lax
from jax.sharding import PartitionSpec as P


def slot_matrix(owner_ids, owners_n, capacity):
    owner = owner_ids[:, 0]
    onehot = (owner[:, None] == jnp.arange(owners_n, dtype=jnp.int32)[None, :]).astype(jnp.int32)
    before = jnp.cumsum(onehot, axis=0) - onehot
    rank = jnp.sum(before * onehot, axis=1)
    slot = owner * capacity + rank
    slots = jnp.arange(owners_n * capacity, dtype=jnp.int32)
    return (slots[:, None] == slot[None, :]).astype(jnp.bfloat16)


def xor_pairs(count, mask):
    return [(s, s ^ mask) for s in range(count)]


def on_device(features, owner_ids, test_blocks):
    owners_n = lax.axis_size("rows")
    blocks_n = lax.axis_size("blk")
    local_rows = features.shape[1]
    width = test_blocks.shape[1]
    capacity = 2 * local_rows // owners_n
    chunk = features.shape[2] // owners_n
    here = lax.axis_index("rows")
    block = lax.axis_index("blk")

    def term(offset, size, tests):
        part = lax.dynamic_slice_in_dim(features, offset, size, axis=2)
        return jnp.einsum("rsk,rtk->st", part, tests, preferred_element_type=jnp.float32)

    chip_bits = [1 << i for i in range(1, owners_n.bit_length() - 1)]
    paired = len(chip_bits) == 2
    if paired:
        core = here % 2
        twin = ((here // 2) ^ (here // 4)) % 2
        pair = 2 * core + twin
        piece = lax.dynamic_slice_in_dim(test_blocks, pair * 2 * chunk, 2 * chunk, axis=2)
    else:
        piece = lax.dynamic_slice_in_dim(test_blocks, here * chunk, chunk, axis=2)
    arrived = []
    for step in range(1, blocks_n):
        pairs = [(b, (b - step) % blocks_n) for b in range(blocks_n)]
        arrived.append(lax.ppermute(piece, "blk", pairs))
    mine = jnp.concatenate(arrived, axis=1)
    own = jnp.einsum("rsk,rtk->st", features, test_blocks, preferred_element_type=jnp.float32)
    slotting = slot_matrix(owner_ids, owners_n, capacity)
    mine, own, slotting = lax.optimization_barrier((mine, own, slotting))
    if paired:
        bx, by = chip_bits
        other = 2 * core + 1 - twin
        remote = term(pair * 2 * chunk, 2 * chunk, mine)
        along_x = lax.ppermute(mine[:, :, :chunk], "rows", xor_pairs(owners_n, bx))
        along_y = lax.ppermute(mine[:, :, chunk:], "rows", xor_pairs(owners_n, by))
        remote = remote + term(other * 2 * chunk, chunk, along_x)
        remote = remote + term(other * 2 * chunk + chunk, chunk, along_y)
        sibling = xor_pairs(owners_n, 1)
        far = 2 * (1 - core) + twin
        near = 2 * (1 - core) + 1 - twin
        remote = remote + term(far * 2 * chunk, 2 * chunk, lax.ppermute(mine, "rows", sibling))
        remote = remote + term(near * 2 * chunk, chunk, lax.ppermute(along_x, "rows", sibling))
        remote = remote + term(near * 2 * chunk + chunk, chunk, lax.ppermute(along_y, "rows", sibling))
    else:
        remote = term(here * chunk, chunk, mine)
        held = mine[None]
        masks = [0]
        for mask in chip_bits:
            got = lax.ppermute(held, "rows", xor_pairs(owners_n, mask))
            for j, m in enumerate(masks):
                remote = remote + term((here ^ mask ^ m) * chunk, chunk, got[j])
            held = jnp.concatenate([held, got], axis=0)
            masks = masks + [m ^ mask for m in masks]
        if owners_n > 1:
            got = lax.ppermute(held, "rows", xor_pairs(owners_n, 1))
            for j, m in enumerate(masks):
                remote = remote + term((here ^ 1 ^ m) * chunk, chunk, got[j])
    relative = jnp.concatenate([own, remote], axis=1)
    doubled = jnp.concatenate([relative, relative], axis=1)
    start = ((blocks_n - block) % blocks_n) * width
    total = lax.dynamic_slice_in_dim(doubled, start, blocks_n * width, axis=1)
    row_scores = total.astype(jnp.bfloat16)
    placed = jnp.dot(
        slotting, row_scores, preferred_element_type=jnp.float32
    ).astype(jnp.bfloat16)
    return lax.all_to_all(placed, "rows", split_axis=0, concat_axis=0, tiled=True)


def solution(mesh):
    return jax.shard_map(
        on_device,
        mesh=mesh,
        in_specs=(P(None, ("blk", "rows"), None), P(("blk", "rows"), None), P(None, "blk", None)),
        out_specs=P(("blk", "rows"), None),
        check_vma=False,
    )
```

```python
import jax
import jax.numpy as jnp
from jax import lax
from jax.sharding import PartitionSpec as P


def slot_matrix(owner_ids, owners_n, capacity):
    owner = owner_ids[:, 0]
    onehot = (owner[:, None] == jnp.arange(owners_n, dtype=jnp.int32)[None, :]).astype(jnp.int32)
    before = jnp.cumsum(onehot, axis=0) - onehot
    rank = jnp.sum(before * onehot, axis=1)
    slot = owner * capacity + rank
    slots = jnp.arange(owners_n * capacity, dtype=jnp.int32)
    return (slots[:, None] == slot[None, :]).astype(jnp.bfloat16)


def xor_pairs(count, mask):
    return [(s, s ^ mask) for s in range(count)]


def on_device(features, owner_ids, test_blocks):
    owners_n = lax.axis_size("rows")
    blocks_n = lax.axis_size("blk")
    local_rows = features.shape[1]
    width = test_blocks.shape[1]
    capacity = 2 * local_rows // owners_n
    chunk = features.shape[2] // owners_n
    here = lax.axis_index("rows")
    block = lax.axis_index("blk")

    def term(offset, size, tests):
        part = lax.dynamic_slice_in_dim(features, offset, size, axis=2)
        return jnp.einsum("rsk,rtk->st", part, tests, preferred_element_type=jnp.float32)

    piece = lax.dynamic_slice_in_dim(test_blocks, here * chunk, chunk, axis=2)
    own = jnp.einsum("rsk,rtk->st", features, test_blocks, preferred_element_type=jnp.float32)
    piece, own = lax.optimization_barrier((piece, own))
    arrived = []
    for step in range(1, blocks_n):
        pairs = [(b, (b - step) % blocks_n) for b in range(blocks_n)]
        arrived.append(lax.ppermute(piece, "blk", pairs))
    mine = jnp.concatenate(arrived, axis=1)
    slotting = slot_matrix(owner_ids, owners_n, capacity)
    mine, own, slotting = lax.optimization_barrier((mine, own, slotting))
    remote = term(here * chunk, chunk, mine)
    chip_bits = [1 << i for i in range(1, owners_n.bit_length() - 1)]
    if len(chip_bits) == 2:
        bx, by = chip_bits
        along_x = lax.ppermute(mine, "rows", xor_pairs(owners_n, bx))
        along_y = lax.ppermute(mine, "rows", xor_pairs(owners_n, by))
        remote = remote + term((here ^ bx) * chunk, chunk, along_x)
        remote = remote + term((here ^ by) * chunk, chunk, along_y)
        half = chunk // 2
        first = lax.ppermute(along_y[:, :, :half], "rows", xor_pairs(owners_n, bx))
        second = lax.ppermute(along_x[:, :, half:], "rows", xor_pairs(owners_n, by))
        corner = (here ^ bx ^ by) * chunk
        remote = remote + term(corner, half, first) + term(corner + half, half, second)
        sibling = xor_pairs(owners_n, 1)
        for mask, got in ((0, mine), (bx, along_x), (by, along_y)):
            remote = remote + term((here ^ 1 ^ mask) * chunk, chunk, lax.ppermute(got, "rows", sibling))
        far = (here ^ 1 ^ bx ^ by) * chunk
        remote = remote + term(far, half, lax.ppermute(first, "rows", sibling))
        remote = remote + term(far + half, half, lax.ppermute(second, "rows", sibling))
    else:
        held = mine[None]
        masks = [0]
        for mask in chip_bits:
            got = lax.ppermute(held, "rows", xor_pairs(owners_n, mask))
            for j, m in enumerate(masks):
                remote = remote + term((here ^ mask ^ m) * chunk, chunk, got[j])
            held = jnp.concatenate([held, got], axis=0)
            masks = masks + [m ^ mask for m in masks]
        if owners_n > 1:
            got = lax.ppermute(held, "rows", xor_pairs(owners_n, 1))
            for j, m in enumerate(masks):
                remote = remote + term((here ^ 1 ^ m) * chunk, chunk, got[j])
    relative = jnp.concatenate([own, remote], axis=1)
    doubled = jnp.concatenate([relative, relative], axis=1)
    start = ((blocks_n - block) % blocks_n) * width
    total = lax.dynamic_slice_in_dim(doubled, start, blocks_n * width, axis=1)
    row_scores = total.astype(jnp.bfloat16)
    placed = jnp.dot(
        slotting, row_scores, preferred_element_type=jnp.float32
    ).astype(jnp.bfloat16)
    return lax.all_to_all(placed, "rows", split_axis=0, concat_axis=0, tiled=True)


def solution(mesh):
    return jax.shard_map(
        on_device,
        mesh=mesh,
        in_specs=(P(None, ("blk", "rows"), None), P(("blk", "rows"), None), P(None, "blk", None)),
        out_specs=P(("blk", "rows"), None),
        check_vma=False,
    )
```
